512 devices in a mesh: lon: 32 (over y_lo, z), lat: 16 (over y_hi, x, core).
Axes of the slice: x: 4, y: 4 (y_hi: 2, y_lo: 2; y = y_hi * 2 + y_lo), z: 16, core: 2. Of those that a mesh axis runs over, the one named last changes fastest.
Arguments:
- tracers: float32 [5, 75, 128, 4096], P(None, None, 'lat', 'lon'), may hold values from -6 to 6
- courant: float32 [2, 75, 128, 4096], P(None, None, 'lat', 'lon'), may hold values from -0.25 to 0.25
- diffusivity: float32 [75], replicated, may hold values from 0.02 to 0.12
- melt_coef: float32 [5], replicated, may hold values from -1 to 1
- berg_profile: float32 [75, 196608], P(None, ('lon', 'lat')), may hold values from 0.05 to 0.5
- berg_mass: float32 [196608], P(('lon', 'lat')), may hold values from 1 to 16
- berg_cell: int32 [2, 196608], P(None, ('lon', 'lat')), may hold values from 0 to 1023
- send_east: int32 [2, 16384], P(None, ('lon', 'lat')), may hold values from 0 to 383, as said below
- send_west: int32 [2, 16384], P(None, ('lon', 'lat')), may hold values from 0 to 383, as said below
Outputs:
- tracers_out: float32 [5, 75, 128, 4096], P(None, None, 'lat', 'lon')
- mass_out: float32 [196608], P(('lon', 'lat'))
The draws below stay inside these ranges and needn't reach their ends.
Inputs may be any that keep to these rules, and one draw needn't show every extreme that they name: In each step, the 32 entries of one block in send_east and its 32 entries in send_west are all different slots of that block. `send_west`: different from the same block's send_east entries of that step, and from each other.
All inputs are finite; a program needn't handle non-finite values.
Results may differ from the reference program's by a relative error of at most 0.0001.
Values sent between devices are 32-bit elements; how exact they have to be, the bound alone decides.
No kernel may reach another device: no remote copies, remote signals or barrier semaphores. Data moves between devices by JAX's collectives and lax.ppermute only.
A program may use at most 64 MiB of HBM per device.

```python
import math
import jax
import jax.numpy as jnp
from jax import lax

FIELDS = 5
LEV = 75
CLAT = 8
CLON = 128
BERG_DEV = 384
CROSS = 32
STEPS = 2
LAT_ALL = 128
LON_ALL = 4096
BERGS = 196608
CELLS = 1024
N_LON = 32
N_LAT = 16
DEVICES = 512


def crossing_order(key):
    scores = jax.random.randint(jax.random.fold_in(key, 7), (STEPS, DEVICES, BERG_DEV), 0, 65536)
    scores = scores * BERG_DEV + jnp.arange(BERG_DEV, dtype=jnp.int32)
    return jnp.argsort(scores, axis=-1).astype(jnp.int32)


def draw_send_east(key, part):
    order = crossing_order(key)
    return order[:, :, :CROSS].reshape(STEPS, DEVICES * CROSS)


def draw_send_west(key, part):
    order = crossing_order(key)
    return order[:, :, CROSS:2 * CROSS].reshape(STEPS, DEVICES * CROSS)


def place_ends(values, key, least, high):
    dims = values.shape
    place = [jax.random.randint(jax.random.fold_in(key, axis), (), 0, dims[axis]) for axis in range(len(dims))]
    values = values.at[tuple(place)].set(least)
    longest = dims.index(max(dims))
    place[longest] = (place[longest] + 1) % dims[longest]
    return values.at[tuple(place)].set(high)


def block_scale(rng, dims, shards, smallest, high):
    level = 1.0
    for position, parts in shards:
        draws = jax.random.uniform(jax.random.fold_in(jax.random.fold_in(rng, 6), position), (parts,), jnp.float32, smallest / len(shards), high / len(shards))
        level = level * jnp.repeat(jnp.exp(draws), dims[position] // parts).reshape((-1,) + (1,) * (len(dims) - 1 - position))
    return level


def gaussian(own_key, shape, spread, bound, pieces=(), kind=jnp.bfloat16):
    gain = block_scale(own_key, shape, pieces, -0.22, 0.18) if pieces else 1.0
    result = jax.random.normal(own_key, shape, jnp.float32) * spread * gain
    return jnp.minimum(jnp.maximum(result, -bound), bound).astype(kind)


def setup_inputs(seed: int = 0) -> dict:
    seeds = jax.random.split(jax.random.key(seed), 10)
    tracers = gaussian(seeds[0], (FIELDS, LEV, LAT_ALL, LON_ALL), 1.0, 6.0, ((2, 16), (3, 32)), jnp.float32)
    courant = jnp.clip(jax.random.uniform(seeds[1], (2, LEV, LAT_ALL, LON_ALL), jnp.float32, -0.25, 0.25) * block_scale(seeds[1], (2, LEV, LAT_ALL, LON_ALL), ((2, 16), (3, 32)), -0.4, 0.0), -0.25, 0.25)
    diffusivity = jnp.clip(jnp.exp(jax.random.uniform(seeds[2], (LEV,), jnp.float32, math.log(0.02), math.log(0.12))), 0.02, 0.12)
    melt_coef = jnp.clip(jax.random.uniform(seeds[3], (FIELDS,), jnp.float32, -1.0, 1.0), -1.0, 1.0)
    berg_profile = jnp.clip(jnp.exp(math.log(0.5) - 2.3025851 * jax.random.uniform(seeds[4], (LEV, BERGS), jnp.float32) ** block_scale(seeds[4], (LEV, BERGS), ((1, 512),), -0.2, 0.2)), 0.05, 0.5)
    berg_mass = jnp.clip(jnp.exp(math.log(16.0) - 2.7725887 * jax.random.uniform(seeds[5], (BERGS,), jnp.float32) ** block_scale(seeds[5], (BERGS,), ((0, 512),), -0.2, 0.2)), 1.0, 16.0)
    berg_cell = place_ends(jax.random.randint(seeds[6], (STEPS, BERGS), 0, CELLS), jax.random.fold_in(seeds[6], 1), 0, CELLS - 1).astype(jnp.int32)
    send_east = draw_send_east(jax.random.fold_in(seeds[9], 71), 0)
    send_west = draw_send_west(jax.random.fold_in(seeds[9], 71), 0)
    return {"tracers": tracers, "courant": courant, "diffusivity": diffusivity, "melt_coef": melt_coef, "berg_profile": berg_profile, "berg_mass": berg_mass, "berg_cell": berg_cell, "send_east": send_east, "send_west": send_west}


def reference(tracers, courant, diffusivity, melt_coef, berg_profile, berg_mass, berg_cell, send_east, send_west):
    records = jnp.concatenate([berg_profile, berg_mass[None, :]], axis=0)
    records = records.reshape(LEV + 1, N_LON, N_LAT, BERG_DEV)
    cells_all = berg_cell.reshape(STEPS, N_LON, N_LAT, BERG_DEV)
    east_all = send_east.reshape(STEPS, N_LON, N_LAT, CROSS)
    west_all = send_west.reshape(STEPS, N_LON, N_LAT, CROSS)
    lon_index = jnp.arange(N_LON, dtype=jnp.int32)[:, None, None]
    lat_index = jnp.arange(N_LAT, dtype=jnp.int32)[None, :, None]
    state = tracers
    east_vel = courant[0]
    north_vel = courant[1]
    west_vel = jnp.roll(east_vel, 1, axis=2)
    south_vel = jnp.concatenate([jnp.zeros_like(north_vel[:, :1, :]), north_vel[:, :-1, :]], axis=1)
    for step_index in range(STEPS):
        east_slots = east_all[step_index]
        west_slots = west_all[step_index]
        east_out = records[:, lon_index, lat_index, east_slots]
        west_out = records[:, lon_index, lat_index, west_slots]
        records = records.at[:, lon_index, lat_index, east_slots].set(jnp.roll(east_out, 1, axis=1))
        records = records.at[:, lon_index, lat_index, west_slots].set(jnp.roll(west_out, -1, axis=1))
        profile = records[:LEV]
        mass_now = records[LEV]
        berg_cells = cells_all[step_index]
        row_pos = lat_index * CLAT + berg_cells // CLON
        col_pos = lon_index * CLON + berg_cells % CLON
        water_temp = state[0][:, row_pos, col_pos]
        melt_rate = profile * jax.nn.softplus(water_temp + 1.8) * jnp.sqrt(mass_now)[None]
        source = jnp.zeros((LEV, LAT_ALL, LON_ALL), jnp.float32).at[:, row_pos, col_pos].add(melt_rate)
        mass_new = mass_now / (1.0 + 0.05 * lax.optimization_barrier(jnp.sum(melt_rate, axis=0)))
        east_side = jnp.roll(state, -1, axis=3)
        west_side = jnp.roll(state, 1, axis=3)
        zero_row = jnp.zeros_like(state[:, :, :1, :])
        north_side = jnp.concatenate([state[:, :, 1:, :], zero_row], axis=2)
        south_side = jnp.concatenate([zero_row, state[:, :, :-1, :]], axis=2)
        flux_east = jnp.maximum(east_vel, 0.0) * state + jnp.minimum(east_vel, 0.0) * east_side
        flux_west = jnp.maximum(west_vel, 0.0) * west_side + jnp.minimum(west_vel, 0.0) * state
        flux_north = jnp.maximum(north_vel, 0.0) * state + jnp.minimum(north_vel, 0.0) * north_side
        flux_south = jnp.maximum(south_vel, 0.0) * south_side + jnp.minimum(south_vel, 0.0) * state
        mixing = east_side + west_side + north_side + south_side - 4.0 * state
        state = state - (flux_east - flux_west) - (flux_north - flux_south) + diffusivity[None, :, None, None] * mixing + melt_coef[:, None, None, None] * source[None]
        records = jnp.concatenate([profile, mass_new[None]], axis=0)
    return (state, records[LEV].reshape(BERGS))
```

```python
import functools

import jax
import jax.numpy as jnp
from jax import lax
from jax.experimental import pallas as pl
from jax.experimental.pallas import tpu as pltpu
from jax.sharding import PartitionSpec as P

STEPS = 2
HI = lax.Precision.HIGHEST
LANES = 128


def _selector(rows):
    r = lax.broadcasted_iota(jnp.int32, (rows, LANES), 0)
    c = lax.broadcasted_iota(jnp.int32, (rows, LANES), 1)
    return jnp.where(((r == 0) & (c == 0)) | ((r == 1) & (c == LANES - 1)), 1.0, 0.0).astype(jnp.float32)


def _columns(block):
    return lax.dot_general(_selector(8), block, (((1,), (1,)), ((), ())), precision=HI,
                           preferred_element_type=jnp.float32)


def _column_matrix(west, east):
    count = west.shape[-1]
    stack = jnp.concatenate([west, east, jnp.zeros((6, count), jnp.float32)], axis=0)
    return lax.dot_general(stack, _selector(8), (((0,), (0,)), ((), ())), precision=HI,
                           preferred_element_type=jnp.float32)


def _extract_kernel(x_ref, c_ref, sn_ref, ss_ref, se_ref, sw_ref):
    fields = x_ref.shape[0]
    levels = sn_ref.shape[1]
    for f in range(fields):
        block = x_ref[f]
        cols = _columns(block)
        se_ref[f:f + 1, :] = cols[1:2]
        sw_ref[f:f + 1, :] = cols[0:1]
        sn_ref[f] = x_ref[f, pl.ds(7, levels, stride=8), :]
        ss_ref[f] = x_ref[f, pl.ds(0, levels, stride=8), :]
    ucols = _columns(c_ref[0])
    se_ref[fields:fields + 1, :] = ucols[1:2]
    sn_ref[fields] = c_ref[1, pl.ds(7, levels, stride=8), :]


def _step_kernel(with_sends, coef_ref, d_ref, x_ref, c_ref, src_ref, fn_ref, fs_ref, fw_ref, fe_ref,
                 cs_ref, cw_ref, o_ref, *rest):
    if with_sends:
        sn_ref, ss_ref, se_ref, sw_ref, hscr = rest
    else:
        (hscr,) = rest
    fields = x_ref.shape[0]
    count = x_ref.shape[1]
    levels = count // 8
    rows = lax.broadcasted_iota(jnp.int32, (count, LANES), 0) % 8
    lanes = lax.broadcasted_iota(jnp.int32, (count, LANES), 1)
    u = c_ref[0]
    v = c_ref[1]
    d = d_ref[...]
    cw = cw_ref.shape[0] - 1
    zero_row = jnp.zeros((1, count), jnp.float32)
    u_halo = _column_matrix(cw_ref[cw:cw + 1, :], zero_row)
    u_w = jnp.where(lanes == 0, u_halo, pltpu.roll(u, 1, 1))
    hscr[pl.ds(0, levels, stride=8), :] = cs_ref[cs_ref.shape[0] - 1]
    v_s = jnp.where(rows == 0, hscr[...], pltpu.roll(v, 1, 0))
    a_c = 1.0 - jnp.maximum(u, 0.0) + jnp.minimum(u_w, 0.0) - jnp.maximum(v, 0.0) + jnp.minimum(v_s, 0.0) - 4.0 * d
    a_e = d - jnp.minimum(u, 0.0)
    a_w = d + jnp.maximum(u_w, 0.0)
    a_n = d - jnp.minimum(v, 0.0)
    a_s = d + jnp.maximum(v_s, 0.0)
    src = src_ref[...]
    for f in range(fields):
        c = x_ref[f]
        halo = _column_matrix(fw_ref[f:f + 1, :], fe_ref[f:f + 1, :])
        east = jnp.where(lanes == LANES - 1, halo, pltpu.roll(c, LANES - 1, 1))
        west = jnp.where(lanes == 0, halo, pltpu.roll(c, 1, 1))
        hscr[pl.ds(7, levels, stride=8), :] = fn_ref[f]
        hscr[pl.ds(0, levels, stride=8), :] = fs_ref[f]
        hrow = hscr[...]
        north = jnp.where(rows == 7, hrow, pltpu.roll(c, count - 1, 0))
        south = jnp.where(rows == 0, hrow, pltpu.roll(c, 1, 0))
        out = a_c * c + a_e * east + a_w * west + a_n * north + a_s * south + coef_ref[f] * src
        o_ref[f] = out
        if with_sends:
            cols = _columns(out)
            se_ref[f:f + 1, :] = cols[1:2]
            sw_ref[f:f + 1, :] = cols[0:1]
            sn_ref[f] = o_ref[f, pl.ds(7, levels, stride=8), :]
            ss_ref[f] = o_ref[f, pl.ds(0, levels, stride=8), :]


def _vmem():
    return pl.BlockSpec(memory_space=pltpu.VMEM)


def extract(x, c):
    fields, count, _ = x.shape
    levels = count // 8
    return pl.pallas_call(
        _extract_kernel,
        out_shape=(
            jax.ShapeDtypeStruct((fields + 1, levels, LANES), jnp.float32),
            jax.ShapeDtypeStruct((fields, levels, LANES), jnp.float32),
            jax.ShapeDtypeStruct((fields + 1, count), jnp.float32),
            jax.ShapeDtypeStruct((fields, count), jnp.float32),
        ),
        in_specs=[_vmem(), _vmem()],
        out_specs=(_vmem(), _vmem(), _vmem(), _vmem()),
    )(x, c)


def step(with_sends, coef, d, x, c, src, fn, fs, fw, fe, cs, cw):
    fields, count, _ = x.shape
    levels = count // 8
    outs = [jax.ShapeDtypeStruct(x.shape, jnp.float32)]
    if with_sends:
        outs += [
            jax.ShapeDtypeStruct((fields, levels, LANES), jnp.float32),
            jax.ShapeDtypeStruct((fields, levels, LANES), jnp.float32),
            jax.ShapeDtypeStruct((fields, count), jnp.float32),
            jax.ShapeDtypeStruct((fields, count), jnp.float32),
        ]
    return pl.pallas_call(
        functools.partial(_step_kernel, with_sends),
        out_shape=tuple(outs),
        in_specs=[pl.BlockSpec(memory_space=pltpu.SMEM)] + [_vmem()] * 10,
        out_specs=tuple(_vmem() for _ in outs),
        scratch_shapes=[pltpu.VMEM((count, LANES), jnp.float32)],
    )(coef, d, x, c, src, fn, fs, fw, fe, cs, cw)


def shift(value, axis, steps, periodic):
    count = lax.axis_size(axis)
    if periodic:
        pairs = [(s, (s + steps) % count) for s in range(count)]
    else:
        pairs = [(s, s + steps) for s in range(count) if 0 <= s + steps < count]
    return lax.ppermute(value, axis, pairs)


def per_device(tracers, courant, diffusivity, melt_coef, berg_profile, berg_mass, berg_cell,
               send_east, send_west):
    fields, levels, rows, cols = tracers.shape
    count = levels * rows
    x = tracers.reshape(fields, count, cols)
    c = courant.reshape(2, count, cols)
    d = jnp.broadcast_to(diffusivity[:, None, None], (levels, rows, cols)).reshape(count, cols)
    records = jnp.concatenate([berg_profile, berg_mass[None, :]], axis=0)
    sn, ss, se, sw = extract(x, c)
    cs = cw = None
    for step_index in range(STEPS):
        east_slots = send_east[step_index]
        west_slots = send_west[step_index]
        east_out = records[:, east_slots]
        west_out = records[:, west_slots]
        from_s = shift(sn, "lat", 1, False)
        from_n = shift(ss, "lat", -1, False)
        from_w = shift(se, "lon", 1, True)
        from_e = shift(sw, "lon", -1, True)
        east_in = shift(east_out, "lon", 1, True)
        west_in = shift(west_out, "lon", -1, True)
        if cs is None:
            cs, cw = from_s, from_w
        records = records.at[:, east_slots].set(east_in)
        records = records.at[:, west_slots].set(west_in)
        profile = records[:levels]
        mass_now = records[levels]
        berg_cells = berg_cell[step_index]
        flat_temp = x[0].reshape(levels, rows * cols)
        water_temp = flat_temp[:, berg_cells]
        melt_rate = profile * jax.nn.softplus(water_temp + 1.8) * jnp.sqrt(mass_now)[None]
        source = jnp.zeros((levels, rows * cols), jnp.float32).at[:, berg_cells].add(melt_rate)
        mass_new = mass_now / (1.0 + 0.05 * jnp.sum(melt_rate, axis=0))
        src = source.reshape(count, cols)
        last = step_index == STEPS - 1
        result = step(not last, melt_coef, d, x, c, src, from_n, from_s, from_w, from_e, cs, cw)
        if last:
            x = result[0]
        else:
            x, sn, ss, se, sw = result
        records = jnp.concatenate([profile, mass_new[None]], axis=0)
    return (x.reshape(fields, levels, rows, cols), records[levels])


def solution(mesh):
    in_specs = (
        P(None, None, "lat", "lon"),
        P(None, None, "lat", "lon"),
        P(),
        P(),
        P(None, ("lon", "lat")),
        P(("lon", "lat")),
        P(None, ("lon", "lat")),
        P(None, ("lon", "lat")),
        P(None, ("lon", "lat")),
    )
    out_specs = (P(None, None, "lat", "lon"), P(("lon", "lat")))
    return jax.shard_map(
        per_device, mesh=mesh, in_specs=in_specs, out_specs=out_specs, check_vma=False
    )
```

```python
import functools

import jax
import jax.numpy as jnp
from jax import lax
from jax.experimental import pallas as pl
from jax.experimental.pallas import tpu as pltpu
from jax.sharding import PartitionSpec as P

STEPS = 2
LANES = 128


def _columns(block, width):
    count = block.shape[0]
    padded = jnp.concatenate([block, jnp.zeros((width - count, LANES), jnp.float32)], axis=0)
    return padded.T


def _column_matrix(west, east, count):
    width = west.shape[-1]
    r = lax.broadcasted_iota(jnp.int32, (LANES, width), 0)
    grid = jnp.where(r == 0, west, jnp.where(r == LANES - 1, east, 0.0))
    return grid.T[:count]


def _extract_kernel(x_ref, c_ref, sn_ref, ss_ref, se_ref, sw_ref):
    fields = x_ref.shape[0]
    levels = sn_ref.shape[1]
    width = se_ref.shape[1]
    for f in range(fields):
        block = x_ref[f]
        cols = _columns(block, width)
        se_ref[f:f + 1, :] = cols[LANES - 1:LANES]
        sw_ref[f:f + 1, :] = cols[0:1]
        sn_ref[f] = x_ref[f, pl.ds(7, levels, stride=8), :]
        ss_ref[f] = x_ref[f, pl.ds(0, levels, stride=8), :]
    ucols = _columns(c_ref[0], width)
    se_ref[fields:fields + 1, :] = ucols[LANES - 1:LANES]
    sn_ref[fields] = c_ref[1, pl.ds(7, levels, stride=8), :]


def _step_kernel(with_sends, coef_ref, d_ref, x_ref, c_ref, src_ref, fn_ref, fs_ref, fw_ref, fe_ref,
                 cs_ref, cw_ref, o_ref, *rest):
    if with_sends:
        sn_ref, ss_ref, se_ref, sw_ref, hscr = rest
    else:
        (hscr,) = rest
    fields = x_ref.shape[0]
    count = x_ref.shape[1]
    levels = count // 8
    rows = lax.broadcasted_iota(jnp.int32, (count, LANES), 0) % 8
    lanes = lax.broadcasted_iota(jnp.int32, (count, LANES), 1)
    u = c_ref[0]
    v = c_ref[1]
    d = d_ref[...]
    width = cw_ref.shape[1]
    zero_row = jnp.zeros((1, width), jnp.float32)
    u_halo = _column_matrix(cw_ref[fields:fields + 1, :], zero_row, count)
    u_w = jnp.where(lanes == 0, u_halo, pltpu.roll(u, 1, 1))
    hscr[pl.ds(0, levels, stride=8), :] = cs_ref[fields]
    v_s = jnp.where(rows == 0, hscr[...], pltpu.roll(v, 1, 0))
    a_c = 1.0 - jnp.maximum(u, 0.0) + jnp.minimum(u_w, 0.0) - jnp.maximum(v, 0.0) + jnp.minimum(v_s, 0.0) - 4.0 * d
    a_e = d - jnp.minimum(u, 0.0)
    a_w = d + jnp.maximum(u_w, 0.0)
    a_n = d - jnp.minimum(v, 0.0)
    a_s = d + jnp.maximum(v_s, 0.0)
    src = src_ref[...]
    for f in range(fields):
        c = x_ref[f]
        halo = _column_matrix(fw_ref[f:f + 1, :], fe_ref[f:f + 1, :], count)
        east = jnp.where(lanes == LANES - 1, halo, pltpu.roll(c, LANES - 1, 1))
        west = jnp.where(lanes == 0, halo, pltpu.roll(c, 1, 1))
        hscr[pl.ds(7, levels, stride=8), :] = fn_ref[f]
        hscr[pl.ds(0, levels, stride=8), :] = fs_ref[f]
        hrow = hscr[...]
        north = jnp.where(rows == 7, hrow, pltpu.roll(c, count - 1, 0))
        south = jnp.where(rows == 0, hrow, pltpu.roll(c, 1, 0))
        out = a_c * c + a_e * east + a_w * west + a_n * north + a_s * south + coef_ref[f] * src
        o_ref[f] = out
        if with_sends:
            cols = _columns(out, width)
            se_ref[f:f + 1, :] = cols[LANES - 1:LANES]
            sw_ref[f:f + 1, :] = cols[0:1]
            sn_ref[f] = o_ref[f, pl.ds(7, levels, stride=8), :]
            ss_ref[f] = o_ref[f, pl.ds(0, levels, stride=8), :]


def _width(count):
    return -(-count // LANES) * LANES


def _vmem():
    return pl.BlockSpec(memory_space=pltpu.VMEM)


def extract(x, c):
    fields, count, _ = x.shape
    levels = count // 8
    return pl.pallas_call(
        _extract_kernel,
        out_shape=(
            jax.ShapeDtypeStruct((fields + 1, levels, LANES), jnp.float32),
            jax.ShapeDtypeStruct((fields, levels, LANES), jnp.float32),
            jax.ShapeDtypeStruct((fields + 1, _width(count)), jnp.float32),
            jax.ShapeDtypeStruct((fields, _width(count)), jnp.float32),
        ),
        in_specs=[_vmem(), _vmem()],
        out_specs=(_vmem(), _vmem(), _vmem(), _vmem()),
    )(x, c)


def step(with_sends, coef, d, x, c, src, fn, fs, fw, fe, cs, cw):
    fields, count, _ = x.shape
    levels = count // 8
    outs = [jax.ShapeDtypeStruct(x.shape, jnp.float32)]
    if with_sends:
        outs += [
            jax.ShapeDtypeStruct((fields, levels, LANES), jnp.float32),
            jax.ShapeDtypeStruct((fields, levels, LANES), jnp.float32),
            jax.ShapeDtypeStruct((fields, _width(count)), jnp.float32),
            jax.ShapeDtypeStruct((fields, _width(count)), jnp.float32),
        ]
    return pl.pallas_call(
        functools.partial(_step_kernel, with_sends),
        out_shape=tuple(outs),
        in_specs=[pl.BlockSpec(memory_space=pltpu.SMEM)] + [_vmem()] * 10,
        out_specs=tuple(_vmem() for _ in outs),
        scratch_shapes=[pltpu.VMEM((count, LANES), jnp.float32)],
    )(coef, d, x, c, src, fn, fs, fw, fe, cs, cw)


def shift(value, axis, steps, periodic):
    count = lax.axis_size(axis)
    if periodic:
        pairs = [(s, (s + steps) % count) for s in range(count)]
    else:
        pairs = [(s, s + steps) for s in range(count) if 0 <= s + steps < count]
    return lax.ppermute(value, axis, pairs)


def with_records(cols, recs):
    flat = recs.reshape(-1)
    width = cols.shape[1]
    rows = -(-flat.size // width)
    flat = jnp.pad(flat, (0, rows * width - flat.size)).reshape(rows, width)
    return jnp.concatenate([cols, flat], axis=0)


def records_of(message, start, shape):
    return message[start:].reshape(-1)[: shape[0] * shape[1]].reshape(shape)


def per_device(tracers, courant, diffusivity, melt_coef, berg_profile, berg_mass, berg_cell,
               send_east, send_west):
    fields, levels, rows, cols = tracers.shape
    count = levels * rows
    x = tracers.reshape(fields, count, cols)
    c = courant.reshape(2, count, cols)
    d = jnp.broadcast_to(diffusivity[:, None, None], (levels, rows, cols)).reshape(count, cols)
    records = jnp.concatenate([berg_profile, berg_mass[None, :]], axis=0)
    sn, ss, se, sw = extract(x, c)
    cs = cw = None
    for step_index in range(STEPS):
        east_slots = send_east[step_index]
        west_slots = send_west[step_index]
        east_out = records[:, east_slots]
        west_out = records[:, west_slots]
        from_s = shift(sn, "lat", 1, False)
        from_n = shift(ss, "lat", -1, False)
        from_w = shift(with_records(se, east_out), "lon", 1, True)
        from_e = shift(with_records(sw, west_out), "lon", -1, True)
        east_in = records_of(from_w, se.shape[0], east_out.shape)
        west_in = records_of(from_e, sw.shape[0], west_out.shape)
        if cs is None:
            cs, cw = from_s, from_w
        records = records.at[:, east_slots].set(east_in)
        records = records.at[:, west_slots].set(west_in)
        profile = records[:levels]
        mass_now = records[levels]
        berg_cells = berg_cell[step_index]
        flat_temp = x[0].reshape(levels, rows * cols)
        water_temp = flat_temp[:, berg_cells]
        melt_rate = profile * jax.nn.softplus(water_temp + 1.8) * jnp.sqrt(mass_now)[None]
        source = jnp.zeros((levels, rows * cols), jnp.float32).at[:, berg_cells].add(melt_rate)
        mass_new = mass_now / (1.0 + 0.05 * jnp.sum(melt_rate, axis=0))
        src = source.reshape(count, cols)
        last = step_index == STEPS - 1
        result = step(not last, melt_coef, d, x, c, src, from_n, from_s, from_w, from_e, cs, cw)
        if last:
            x = result[0]
        else:
            x, sn, ss, se, sw = result
        records = jnp.concatenate([profile, mass_new[None]], axis=0)
    return (x.reshape(fields, levels, rows, cols), records[levels])


def solution(mesh):
    in_specs = (
        P(None, None, "lat", "lon"),
        P(None, None, "lat", "lon"),
        P(),
        P(),
        P(None, ("lon", "lat")),
        P(("lon", "lat")),
        P(None, ("lon", "lat")),
        P(None, ("lon", "lat")),
        P(None, ("lon", "lat")),
    )
    out_specs = (P(None, None, "lat", "lon"), P(("lon", "lat")))
    return jax.shard_map(
        per_device, mesh=mesh, in_specs=in_specs, out_specs=out_specs, check_vma=False
    )
```

```python
import functools

import jax
import jax.numpy as jnp
from jax import lax
from jax.experimental import pallas as pl
from jax.experimental.pallas import tpu as pltpu
from jax.sharding import PartitionSpec as P

STEPS = 2
LANES = 128
HI = lax.Precision.HIGHEST
REC_ROW = 32
MSG_ROWS = 112


def _dot(a, b, dims):
    return lax.dot_general(a, b, (dims, ((), ())), precision=HI, preferred_element_type=jnp.float32)


def _pieces(count):
    return -(-count // LANES)


def _columns(block):
    count = block.shape[0]
    width = _pieces(count) * LANES
    padded = jnp.concatenate([block, jnp.zeros((width - count, LANES), jnp.float32)], axis=0)
    return padded.T


def _put_column(msg_ref, slot, vector):
    pieces = vector.shape[1] // LANES
    for j in range(pieces):
        row = slot * pieces + j
        msg_ref[row:row + 1, :] = vector[:, j * LANES:(j + 1) * LANES]


def _get_column(msg_ref, slot, pieces):
    return jnp.concatenate(
        [msg_ref[slot * pieces + j:slot * pieces + j + 1, :] for j in range(pieces)], axis=1)


def _column_matrix(west, east, count):
    width = west.shape[-1]
    r = lax.broadcasted_iota(jnp.int32, (LANES, width), 0)
    grid = jnp.where(r == 0, west, jnp.where(r == LANES - 1, east, 0.0))
    return grid.T[:count]


def _one_hot(index_row, size):
    n = index_row.shape[1]
    return jnp.where(lax.broadcasted_iota(jnp.int32, (size, n), 0) == index_row, 1.0, 0.0)


def _send_records(msg_ref, prof, mass, index_row):
    slots = prof.shape[1]
    hot = _one_hot(index_row, slots)
    levels = prof.shape[0]
    cross = index_row.shape[1]
    msg_ref[REC_ROW:REC_ROW + levels, 0:cross] = _dot(prof, hot, ((1,), (0,)))
    msg_ref[REC_ROW + levels:REC_ROW + levels + 1, 0:cross] = _dot(mass, hot, ((1,), (0,)))


def _prep_kernel(x_ref, c_ref, p_ref, m_ref, ie_ref, iw_ref, sn_ref, ss_ref, me_ref, mw_ref):
    fields, count, _ = x_ref.shape
    levels = count // 8
    me_ref[...] = jnp.zeros(me_ref.shape, jnp.float32)
    mw_ref[...] = jnp.zeros(mw_ref.shape, jnp.float32)
    for f in range(fields):
        cols = _columns(x_ref[f])
        _put_column(me_ref, f, cols[LANES - 1:LANES])
        _put_column(mw_ref, f, cols[0:1])
        sn_ref[f] = x_ref[f, pl.ds(7, levels, stride=8), :]
        ss_ref[f] = x_ref[f, pl.ds(0, levels, stride=8), :]
    ucols = _columns(c_ref[0])
    _put_column(me_ref, fields, ucols[LANES - 1:LANES])
    sn_ref[fields] = c_ref[1, pl.ds(7, levels, stride=8), :]
    prof = p_ref[...]
    mass = m_ref[...]
    _send_records(me_ref, prof, mass, ie_ref[0:1, :])
    _send_records(mw_ref, prof, mass, iw_ref[0:1, :])


def _step_kernel(step_index, with_sends, coef_ref, d_ref, x_ref, c_ref, p_ref, m_ref, cell_ref,
                 ie_ref, iw_ref, fn_ref, fs_ref, fw_ref, fe_ref, cs_ref, cw_ref, *rest):
    if with_sends:
        o_ref, po_ref, mo_ref, sn_ref, ss_ref, me_ref, mw_ref, hscr, sscr, dscr = rest
    else:
        o_ref, po_ref, mo_ref, hscr, sscr, dscr = rest
    fields, count, _ = x_ref.shape
    levels = count // 8
    pieces = _pieces(count)
    slots = p_ref.shape[1]
    cross = ie_ref.shape[1]
    cells = 8 * LANES

    hot_e = _one_hot(ie_ref[step_index:step_index + 1, :], slots)
    hot_w = _one_hot(iw_ref[step_index:step_index + 1, :], slots)
    rec_e = fw_ref[REC_ROW:REC_ROW + levels + 1, 0:cross]
    rec_w = fe_ref[REC_ROW:REC_ROW + levels + 1, 0:cross]
    placed = _dot(rec_e, hot_e, ((1,), (1,))) + _dot(rec_w, hot_w, ((1,), (1,)))
    taken = _dot(jnp.ones((8, cross), jnp.float32), hot_e + hot_w, ((1,), (1,)))[0:1]
    moved = taken > 0.5
    prof = jnp.where(moved, placed[:levels], p_ref[...])
    mass = jnp.where(moved, placed[levels:levels + 1], m_ref[...])

    temp = jnp.concatenate([x_ref[0, pl.ds(r, levels, stride=8), :] for r in range(8)], axis=1)
    hot_c = _one_hot(cell_ref[step_index:step_index + 1, :], cells)
    water = _dot(temp, hot_c, ((1,), (0,)))
    z = water + 1.8
    soft = jnp.maximum(z, 0.0) + jnp.log1p(jnp.exp(-jnp.abs(z)))
    melt = prof * soft * jnp.sqrt(mass)
    source = _dot(melt, hot_c, ((1,), (1,)))
    mass_new = mass / (1.0 + 0.05 * jnp.sum(melt, axis=0, keepdims=True))
    po_ref[...] = prof
    mo_ref[...] = mass_new
    for r in range(8):
        sscr[pl.ds(r, levels, stride=8), :] = source[:, r * LANES:(r + 1) * LANES]
        dscr[pl.ds(r, levels, stride=8), :] = jnp.broadcast_to(d_ref[...], (levels, LANES))

    rows = lax.broadcasted_iota(jnp.int32, (count, LANES), 0) % 8
    lanes = lax.broadcasted_iota(jnp.int32, (count, LANES), 1)
    u = c_ref[0]
    v = c_ref[1]
    d = dscr[...]
    zero_row = jnp.zeros((1, pieces * LANES), jnp.float32)
    u_halo = _column_matrix(_get_column(cw_ref, fields, pieces), zero_row, count)
    u_w = jnp.where(lanes == 0, u_halo, pltpu.roll(u, 1, 1))
    hscr[pl.ds(0, levels, stride=8), :] = cs_ref[fields]
    v_s = jnp.where(rows == 0, hscr[...], pltpu.roll(v, 1, 0))
    a_c = 1.0 - jnp.maximum(u, 0.0) + jnp.minimum(u_w, 0.0) - jnp.maximum(v, 0.0) + jnp.minimum(v_s, 0.0) - 4.0 * d
    a_e = d - jnp.minimum(u, 0.0)
    a_w = d + jnp.maximum(u_w, 0.0)
    a_n = d - jnp.minimum(v, 0.0)
    a_s = d + jnp.maximum(v_s, 0.0)
    src = sscr[...]
    if with_sends:
        me_ref[...] = jnp.zeros(me_ref.shape, jnp.float32)
        mw_ref[...] = jnp.zeros(mw_ref.shape, jnp.float32)
    for f in range(fields):
        c = x_ref[f]
        halo = _column_matrix(_get_column(fw_ref, f, pieces), _get_column(fe_ref, f, pieces), count)
        east = jnp.where(lanes == LANES - 1, halo, pltpu.roll(c, LANES - 1, 1))
        west = jnp.where(lanes == 0, halo, pltpu.roll(c, 1, 1))
        hscr[pl.ds(7, levels, stride=8), :] = fn_ref[f]
        hscr[pl.ds(0, levels, stride=8), :] = fs_ref[f]
        hrow = hscr[...]
        north = jnp.where(rows == 7, hrow, pltpu.roll(c, count - 1, 0))
        south = jnp.where(rows == 0, hrow, pltpu.roll(c, 1, 0))
        out = a_c * c + a_e * east + a_w * west + a_n * north + a_s * south + coef_ref[f] * src
        o_ref[f] = out
        if with_sends:
            cols = _columns(out)
            _put_column(me_ref, f, cols[LANES - 1:LANES])
            _put_column(mw_ref, f, cols[0:1])
            sn_ref[f] = o_ref[f, pl.ds(7, levels, stride=8), :]
            ss_ref[f] = o_ref[f, pl.ds(0, levels, stride=8), :]
    if with_sends:
        nxt = step_index + 1
        _send_records(me_ref, prof, mass_new, ie_ref[nxt:nxt + 1, :])
        _send_records(mw_ref, prof, mass_new, iw_ref[nxt:nxt + 1, :])


def _vmem():
    return pl.BlockSpec(memory_space=pltpu.VMEM)


def _f32(shape):
    return jax.ShapeDtypeStruct(shape, jnp.float32)


def prep(x, c, prof, mass, ie, iw):
    fields, count, _ = x.shape
    levels = count // 8
    return pl.pallas_call(
        _prep_kernel,
        out_shape=(
            _f32((fields + 1, levels, LANES)),
            _f32((fields, levels, LANES)),
            _f32((MSG_ROWS, LANES)),
            _f32((MSG_ROWS, LANES)),
        ),
        in_specs=[_vmem()] * 6,
        out_specs=tuple(_vmem() for _ in range(4)),
    )(x, c, prof, mass, ie, iw)


def step(step_index, with_sends, coef, d, x, c, prof, mass, cell, ie, iw, fn, fs, fw, fe, cs, cw):
    fields, count, _ = x.shape
    levels = count // 8
    outs = [_f32(x.shape), _f32(prof.shape), _f32(mass.shape)]
    if with_sends:
        outs += [
            _f32((fields, levels, LANES)),
            _f32((fields, levels, LANES)),
            _f32((MSG_ROWS, LANES)),
            _f32((MSG_ROWS, LANES)),
        ]
    return pl.pallas_call(
        functools.partial(_step_kernel, step_index, with_sends),
        out_shape=tuple(outs),
        in_specs=[pl.BlockSpec(memory_space=pltpu.SMEM)] + [_vmem()] * 14,
        out_specs=tuple(_vmem() for _ in outs),
        scratch_shapes=[pltpu.VMEM((count, LANES), jnp.float32)] * 3,
    )(coef, d, x, c, prof, mass, cell, ie, iw, fn, fs, fw, fe, cs, cw)


def shift(value, axis, steps, periodic):
    count = lax.axis_size(axis)
    if periodic:
        pairs = [(s, (s + steps) % count) for s in range(count)]
    else:
        pairs = [(s, s + steps) for s in range(count) if 0 <= s + steps < count]
    return lax.ppermute(value, axis, pairs)


def per_device(tracers, courant, diffusivity, melt_coef, berg_profile, berg_mass, berg_cell,
               send_east, send_west):
    fields, levels, rows, cols = tracers.shape
    count = levels * rows
    x = tracers.reshape(fields, count, cols)
    c = courant.reshape(2, count, cols)
    d = diffusivity.reshape(levels, 1)
    prof = berg_profile
    mass = berg_mass.reshape(1, -1)
    sn, ss, me, mw = prep(x, c, prof, mass, send_east, send_west)
    cs = cw = None
    for step_index in range(STEPS):
        from_s = shift(sn, "lat", 1, False)
        from_n = shift(ss, "lat", -1, False)
        from_w = shift(me, "lon", 1, True)
        from_e = shift(mw, "lon", -1, True)
        if cs is None:
            cs, cw = from_s, from_w
        with_sends = step_index < STEPS - 1
        result = step(step_index, with_sends, melt_coef, d, x, c, prof, mass, berg_cell, send_east,
                      send_west, from_n, from_s, from_w, from_e, cs, cw)
        if with_sends:
            x, prof, mass, sn, ss, me, mw = result
        else:
            x, prof, mass = result
    return (x.reshape(fields, levels, rows, cols), mass.reshape(-1))


def solution(mesh):
    in_specs = (
        P(None, None, "lat", "lon"),
        P(None, None, "lat", "lon"),
        P(),
        P(),
        P(None, ("lon", "lat")),
        P(("lon", "lat")),
        P(None, ("lon", "lat")),
        P(None, ("lon", "lat")),
        P(None, ("lon", "lat")),
    )
    out_specs = (P(None, None, "lat", "lon"), P(("lon", "lat")))
    return jax.shard_map(
        per_device, mesh=mesh, in_specs=in_specs, out_specs=out_specs, check_vma=False
    )
```

```python
import functools

import jax
import jax.numpy as jnp
from jax import lax
from jax.experimental import pallas as pl
from jax.experimental.pallas import tpu as pltpu
from jax.sharding import PartitionSpec as P

STEPS = 2
LANES = 128
HI = lax.Precision.HIGHEST
REC_ROW = 32
MSG_ROWS = 112


def _dot(a, b, dims):
    return lax.dot_general(a, b, (dims, ((), ())), precision=HI, preferred_element_type=jnp.float32)


def _pieces(count):
    return -(-count // LANES)


def _columns(block):
    count = block.shape[0]
    width = _pieces(count) * LANES
    padded = jnp.concatenate([block, jnp.zeros((width - count, LANES), jnp.float32)], axis=0)
    return padded.T


def _put_column(msg_ref, slot, vector):
    pieces = vector.shape[1] // LANES
    for j in range(pieces):
        row = slot * pieces + j
        msg_ref[row:row + 1, :] = vector[:, j * LANES:(j + 1) * LANES]


def _get_column(msg_ref, slot, pieces):
    return jnp.concatenate(
        [msg_ref[slot * pieces + j:slot * pieces + j + 1, :] for j in range(pieces)], axis=1)


def _column_matrix(west, east, count):
    width = west.shape[-1]
    r = lax.broadcasted_iota(jnp.int32, (LANES, width), 0)
    grid = jnp.where(r == 0, west, jnp.where(r == LANES - 1, east, 0.0))
    return grid.T[:count]


def _one_hot(index_row, size):
    n = index_row.shape[1]
    return jnp.where(lax.broadcasted_iota(jnp.int32, (size, n), 0) == index_row, 1.0, 0.0)


def _send_records(msg_ref, prof, mass, index_row):
    slots = prof.shape[1]
    hot = _one_hot(index_row, slots)
    levels = prof.shape[0]
    cross = index_row.shape[1]
    msg_ref[REC_ROW:REC_ROW + levels, 0:cross] = _dot(prof, hot, ((1,), (0,)))
    msg_ref[REC_ROW + levels:REC_ROW + levels + 1, 0:cross] = _dot(mass, hot, ((1,), (0,)))


def _prep_kernel(x_ref, c_ref, p_ref, m_ref, ie_ref, iw_ref, sn_ref, ss_ref, me_ref, mw_ref):
    fields, count, _ = x_ref.shape
    levels = count // 8
    me_ref[...] = jnp.zeros(me_ref.shape, jnp.float32)
    mw_ref[...] = jnp.zeros(mw_ref.shape, jnp.float32)
    for f in range(fields):
        cols = _columns(x_ref[f])
        _put_column(me_ref, f, cols[LANES - 1:LANES])
        _put_column(mw_ref, f, cols[0:1])
        sn_ref[f] = x_ref[f, pl.ds(7, levels, stride=8), :]
        ss_ref[f] = x_ref[f, pl.ds(0, levels, stride=8), :]
    ucols = _columns(c_ref[0])
    _put_column(me_ref, fields, ucols[LANES - 1:LANES])
    sn_ref[fields] = c_ref[1, pl.ds(7, levels, stride=8), :]
    prof = p_ref[...]
    mass = m_ref[...].reshape(1, -1)
    _send_records(me_ref, prof, mass, ie_ref[0:1, :])
    _send_records(mw_ref, prof, mass, iw_ref[0:1, :])


def _step_kernel(step_index, with_sends, coef_ref, d_ref, x_ref, c_ref, p_ref, m_ref, cell_ref,
                 ie_ref, iw_ref, fn_ref, fs_ref, fw_ref, fe_ref, cs_ref, cw_ref, *rest):
    if with_sends:
        o_ref, po_ref, mo_ref, sn_ref, ss_ref, me_ref, mw_ref, hscr, sscr, dscr = rest
    else:
        o_ref, po_ref, mo_ref, hscr, sscr, dscr = rest
    fields, count, _ = x_ref.shape
    levels = count // 8
    pieces = _pieces(count)
    slots = p_ref.shape[1]
    cross = ie_ref.shape[1]
    cells = 8 * LANES

    hot_e = _one_hot(ie_ref[step_index:step_index + 1, :], slots)
    hot_w = _one_hot(iw_ref[step_index:step_index + 1, :], slots)
    rec_e = fw_ref[REC_ROW:REC_ROW + levels + 1, 0:cross]
    rec_w = fe_ref[REC_ROW:REC_ROW + levels + 1, 0:cross]
    placed = _dot(rec_e, hot_e, ((1,), (1,))) + _dot(rec_w, hot_w, ((1,), (1,)))
    taken = _dot(jnp.ones((8, cross), jnp.float32), hot_e + hot_w, ((1,), (1,)))[0:1]
    moved = taken > 0.5
    prof = jnp.where(moved, placed[:levels], p_ref[...])
    mass = jnp.where(moved, placed[levels:levels + 1], m_ref[...].reshape(1, -1))

    temp = jnp.concatenate([x_ref[0, pl.ds(r, levels, stride=8), :] for r in range(8)], axis=1)
    hot_c = _one_hot(cell_ref[step_index:step_index + 1, :], cells)
    water = _dot(temp, hot_c, ((1,), (0,)))
    z = water + 1.8
    soft = jnp.maximum(z, 0.0) + jnp.log1p(jnp.exp(-jnp.abs(z)))
    melt = prof * soft * jnp.sqrt(mass)
    source = _dot(melt, hot_c, ((1,), (1,)))
    mass_new = mass / (1.0 + 0.05 * jnp.sum(melt, axis=0, keepdims=True))
    po_ref[...] = prof
    mo_ref[...] = mass_new.reshape(-1)
    for r in range(8):
        sscr[pl.ds(r, levels, stride=8), :] = source[:, r * LANES:(r + 1) * LANES]
    for l in range(levels):
        dscr[l * 8:(l + 1) * 8, :] = jnp.full((8, LANES), d_ref[l], jnp.float32)

    rows = lax.broadcasted_iota(jnp.int32, (count, LANES), 0) % 8
    lanes = lax.broadcasted_iota(jnp.int32, (count, LANES), 1)
    u = c_ref[0]
    v = c_ref[1]
    d = dscr[...]
    zero_row = jnp.zeros((1, pieces * LANES), jnp.float32)
    u_halo = _column_matrix(_get_column(cw_ref, fields, pieces), zero_row, count)
    u_w = jnp.where(lanes == 0, u_halo, pltpu.roll(u, 1, 1))
    hscr[...] = jnp.zeros(hscr.shape, jnp.float32)
    hscr[pl.ds(0, levels, stride=8), :] = cs_ref[fields]
    v_s = jnp.where(rows == 0, hscr[...], pltpu.roll(v, 1, 0))
    a_c = 1.0 - jnp.maximum(u, 0.0) + jnp.minimum(u_w, 0.0) - jnp.maximum(v, 0.0) + jnp.minimum(v_s, 0.0) - 4.0 * d
    a_e = d - jnp.minimum(u, 0.0)
    a_w = d + jnp.maximum(u_w, 0.0)
    a_n = d - jnp.minimum(v, 0.0)
    a_s = d + jnp.maximum(v_s, 0.0)
    last_lane = lanes == LANES - 1
    first_lane = lanes == 0
    top_row = rows == 7
    bottom_row = rows == 0
    a_ew = jnp.where(last_lane, a_e, jnp.where(first_lane, a_w, 0.0))
    a_ns = jnp.where(top_row, a_n, jnp.where(bottom_row, a_s, 0.0))
    a_e = jnp.where(last_lane, 0.0, a_e)
    a_w = jnp.where(first_lane, 0.0, a_w)
    a_n = jnp.where(top_row, 0.0, a_n)
    a_s = jnp.where(bottom_row, 0.0, a_s)
    src = sscr[...]
    if with_sends:
        me_ref[...] = jnp.zeros(me_ref.shape, jnp.float32)
        mw_ref[...] = jnp.zeros(mw_ref.shape, jnp.float32)
    for f in range(fields):
        c = x_ref[f]
        halo = _column_matrix(_get_column(fw_ref, f, pieces), _get_column(fe_ref, f, pieces), count)
        hscr[pl.ds(7, levels, stride=8), :] = fn_ref[f]
        hscr[pl.ds(0, levels, stride=8), :] = fs_ref[f]
        hrow = hscr[...]
        out = (a_c * c + a_e * pltpu.roll(c, LANES - 1, 1) + a_w * pltpu.roll(c, 1, 1)
               + a_n * pltpu.roll(c, count - 1, 0) + a_s * pltpu.roll(c, 1, 0)
               + a_ew * halo + a_ns * hrow + coef_ref[f] * src)
        o_ref[f] = out
        if with_sends:
            cols = _columns(out)
            _put_column(me_ref, f, cols[LANES - 1:LANES])
            _put_column(mw_ref, f, cols[0:1])
            sn_ref[f] = o_ref[f, pl.ds(7, levels, stride=8), :]
            ss_ref[f] = o_ref[f, pl.ds(0, levels, stride=8), :]
    if with_sends:
        nxt = step_index + 1
        _send_records(me_ref, prof, mass_new, ie_ref[nxt:nxt + 1, :])
        _send_records(mw_ref, prof, mass_new, iw_ref[nxt:nxt + 1, :])


def _vmem():
    return pl.BlockSpec(memory_space=pltpu.VMEM)


def _f32(shape):
    return jax.ShapeDtypeStruct(shape, jnp.float32)


def prep(x, c, prof, mass, ie, iw):
    fields, count, _ = x.shape
    levels = count // 8
    return pl.pallas_call(
        _prep_kernel,
        out_shape=(
            _f32((fields + 1, levels, LANES)),
            _f32((fields, levels, LANES)),
            _f32((MSG_ROWS, LANES)),
            _f32((MSG_ROWS, LANES)),
        ),
        in_specs=[_vmem()] * 6,
        out_specs=tuple(_vmem() for _ in range(4)),
    )(x, c, prof, mass, ie, iw)


def step(step_index, with_sends, coef, d, x, c, prof, mass, cell, ie, iw, fn, fs, fw, fe, cs, cw):
    fields, count, _ = x.shape
    levels = count // 8
    outs = [_f32(x.shape), _f32(prof.shape), _f32(mass.shape)]
    if with_sends:
        outs += [
            _f32((fields, levels, LANES)),
            _f32((fields, levels, LANES)),
            _f32((MSG_ROWS, LANES)),
            _f32((MSG_ROWS, LANES)),
        ]
    return pl.pallas_call(
        functools.partial(_step_kernel, step_index, with_sends),
        out_shape=tuple(outs),
        in_specs=[pl.BlockSpec(memory_space=pltpu.SMEM)] * 2 + [_vmem()] * 13,
        out_specs=tuple(_vmem() for _ in outs),
        scratch_shapes=[pltpu.VMEM((count, LANES), jnp.float32)] * 3,
    )(coef, d, x, c, prof, mass, cell, ie, iw, fn, fs, fw, fe, cs, cw)


def shift(value, axis, steps, periodic):
    count = lax.axis_size(axis)
    if periodic:
        pairs = [(s, (s + steps) % count) for s in range(count)]
    else:
        pairs = [(s, s + steps) for s in range(count) if 0 <= s + steps < count]
    return lax.ppermute(value, axis, pairs)


def per_device(tracers, courant, diffusivity, melt_coef, berg_profile, berg_mass, berg_cell,
               send_east, send_west):
    fields, levels, rows, cols = tracers.shape
    count = levels * rows
    x = tracers.reshape(fields, count, cols)
    c = courant.reshape(2, count, cols)
    d = diffusivity
    prof = berg_profile
    mass = berg_mass
    sn, ss, me, mw = prep(x, c, prof, mass, send_east, send_west)
    cs = cw = None
    for step_index in range(STEPS):
        from_s = shift(sn, "lat", 1, False)
        from_n = shift(ss, "lat", -1, False)
        from_w = shift(me, "lon", 1, True)
        from_e = shift(mw, "lon", -1, True)
        if cs is None:
            cs, cw = from_s, from_w
        with_sends = step_index < STEPS - 1
        result = step(step_index, with_sends, melt_coef, d, x, c, prof, mass, berg_cell, send_east,
                      send_west, from_n, from_s, from_w, from_e, cs, cw)
        if with_sends:
            x, prof, mass, sn, ss, me, mw = result
        else:
            x, prof, mass = result
    return (x.reshape(fields, levels, rows, cols), mass)


def solution(mesh):
    in_specs = (
        P(None, None, "lat", "lon"),
        P(None, None, "lat", "lon"),
        P(),
        P(),
        P(None, ("lon", "lat")),
        P(("lon", "lat")),
        P(None, ("lon", "lat")),
        P(None, ("lon", "lat")),
        P(None, ("lon", "lat")),
    )
    out_specs = (P(None, None, "lat", "lon"), P(("lon", "lat")))
    return jax.shard_map(
        per_device, mesh=mesh, in_specs=in_specs, out_specs=out_specs, check_vma=False
    )
```

```python
import functools

import jax
import jax.numpy as jnp
from jax import lax
from jax.experimental import pallas as pl
from jax.experimental.pallas import tpu as pltpu
from jax.sharding import PartitionSpec as P

STEPS = 2
LANES = 128
HI = lax.Precision.HIGHEST
REC_ROW = 32
MSG_ROWS = 112


def _dot(a, b, dims):
    return lax.dot_general(a, b, (dims, ((), ())), precision=HI, preferred_element_type=jnp.float32)


def _split3(a):
    hi = a.astype(jnp.bfloat16)
    rest = a - hi.astype(jnp.float32)
    mid = rest.astype(jnp.bfloat16)
    lo = (rest - mid.astype(jnp.float32)).astype(jnp.bfloat16)
    return jnp.concatenate([hi, mid, lo], axis=0)


def _select(a, hot, dims):
    m = a.shape[0]
    part = lax.dot_general(_split3(a), hot.astype(jnp.bfloat16), (dims, ((), ())),
                           preferred_element_type=jnp.float32)
    return (part[:m] + part[m:2 * m]) + part[2 * m:]


def _pieces(count):
    return -(-count // LANES)


def _columns(block):
    count = block.shape[0]
    width = _pieces(count) * LANES
    padded = jnp.concatenate([block, jnp.zeros((width - count, LANES), jnp.float32)], axis=0)
    return padded.T


def _put_column(msg_ref, slot, vector):
    pieces = vector.shape[1] // LANES
    for j in range(pieces):
        row = slot * pieces + j
        msg_ref[row:row + 1, :] = vector[:, j * LANES:(j + 1) * LANES]


def _get_column(msg_ref, slot, pieces):
    return jnp.concatenate(
        [msg_ref[slot * pieces + j:slot * pieces + j + 1, :] for j in range(pieces)], axis=1)


def _column_matrix(west, east, count):
    width = west.shape[-1]
    r = lax.broadcasted_iota(jnp.int32, (LANES, width), 0)
    grid = jnp.where(r == 0, west, jnp.where(r == LANES - 1, east, 0.0))
    return grid.T[:count]


def _one_hot(index_row, size):
    n = index_row.shape[1]
    return jnp.where(lax.broadcasted_iota(jnp.int32, (size, n), 0) == index_row, 1.0, 0.0)


def _send_records(msg_ref, prof, mass, index_row):
    slots = prof.shape[1]
    hot = _one_hot(index_row, slots)
    levels = prof.shape[0]
    cross = index_row.shape[1]
    rec = _select(jnp.concatenate([prof, mass, jnp.zeros((4, slots), jnp.float32)], axis=0), hot,
                  ((1,), (0,)))
    msg_ref[REC_ROW:REC_ROW + levels + 1, 0:cross] = rec[:levels + 1]


def _prep_kernel(x_ref, c_ref, p_ref, m_ref, ie_ref, iw_ref, sn_ref, ss_ref, me_ref, mw_ref):
    fields, count, _ = x_ref.shape
    levels = count // 8
    me_ref[...] = jnp.zeros(me_ref.shape, jnp.float32)
    mw_ref[...] = jnp.zeros(mw_ref.shape, jnp.float32)
    for f in range(fields):
        cols = _columns(x_ref[f])
        _put_column(me_ref, f, cols[LANES - 1:LANES])
        _put_column(mw_ref, f, cols[0:1])
        sn_ref[f] = x_ref[f, pl.ds(7, levels, stride=8), :]
        ss_ref[f] = x_ref[f, pl.ds(0, levels, stride=8), :]
    ucols = _columns(c_ref[0])
    _put_column(me_ref, fields, ucols[LANES - 1:LANES])
    sn_ref[fields] = c_ref[1, pl.ds(7, levels, stride=8), :]
    prof = p_ref[...]
    mass = m_ref[...].reshape(1, -1)
    _send_records(me_ref, prof, mass, ie_ref[0:1, :])
    _send_records(mw_ref, prof, mass, iw_ref[0:1, :])


def _step_kernel(step_index, with_sends, coef_ref, d_ref, x_ref, c_ref, p_ref, m_ref, cell_ref,
                 ie_ref, iw_ref, fn_ref, fs_ref, fw_ref, fe_ref, cs_ref, cw_ref, *rest):
    if with_sends:
        o_ref, po_ref, mo_ref, sn_ref, ss_ref, me_ref, mw_ref, hscr, sscr, dscr = rest
    else:
        o_ref, po_ref, mo_ref, hscr, sscr, dscr = rest
    fields, count, _ = x_ref.shape
    levels = count // 8
    pieces = _pieces(count)
    slots = p_ref.shape[1]
    cross = ie_ref.shape[1]
    cells = 8 * LANES

    hot_e = _one_hot(ie_ref[step_index:step_index + 1, :], slots)
    hot_w = _one_hot(iw_ref[step_index:step_index + 1, :], slots)
    rec_e = fw_ref[REC_ROW:REC_ROW + levels + 5, 0:cross]
    rec_w = fe_ref[REC_ROW:REC_ROW + levels + 5, 0:cross]
    placed = _select(rec_e, hot_e, ((1,), (1,))) + _select(rec_w, hot_w, ((1,), (1,)))
    taken = lax.dot_general(jnp.ones((8, cross), jnp.bfloat16), (hot_e + hot_w).astype(jnp.bfloat16),
                            (((1,), (1,)), ((), ())), preferred_element_type=jnp.float32)[0:1]
    moved = taken > 0.5
    prof = jnp.where(moved, placed[:levels], p_ref[...])
    mass = jnp.where(moved, placed[levels:levels + 1], m_ref[...].reshape(1, -1))

    temp = jnp.concatenate([x_ref[0, pl.ds(r, levels, stride=8), :] for r in range(8)], axis=1)
    hot_c = _one_hot(cell_ref[step_index:step_index + 1, :], cells)
    water = _select(temp, hot_c, ((1,), (0,)))
    z = water + 1.8
    soft = jnp.maximum(z, 0.0) + jnp.log1p(jnp.exp(-jnp.abs(z)))
    melt = prof * soft * jnp.sqrt(mass)
    source = _select(melt, hot_c, ((1,), (1,)))
    mass_new = mass / (1.0 + 0.05 * jnp.sum(melt, axis=0, keepdims=True))
    po_ref[...] = prof
    mo_ref[...] = mass_new.reshape(-1)
    for r in range(8):
        sscr[pl.ds(r, levels, stride=8), :] = source[:, r * LANES:(r + 1) * LANES]
    for l in range(levels):
        dscr[l * 8:(l + 1) * 8, :] = jnp.full((8, LANES), d_ref[l], jnp.float32)

    rows = lax.broadcasted_iota(jnp.int32, (count, LANES), 0) % 8
    lanes = lax.broadcasted_iota(jnp.int32, (count, LANES), 1)
    u = c_ref[0]
    v = c_ref[1]
    d = dscr[...]
    zero_row = jnp.zeros((1, pieces * LANES), jnp.float32)
    u_halo = _column_matrix(_get_column(cw_ref, fields, pieces), zero_row, count)
    u_w = jnp.where(lanes == 0, u_halo, pltpu.roll(u, 1, 1))
    hscr[...] = jnp.zeros(hscr.shape, jnp.float32)
    hscr[pl.ds(0, levels, stride=8), :] = cs_ref[fields]
    v_s = jnp.where(rows == 0, hscr[...], pltpu.roll(v, 1, 0))
    a_c = 1.0 - jnp.maximum(u, 0.0) + jnp.minimum(u_w, 0.0) - jnp.maximum(v, 0.0) + jnp.minimum(v_s, 0.0) - 4.0 * d
    a_e = d - jnp.minimum(u, 0.0)
    a_w = d + jnp.maximum(u_w, 0.0)
    a_n = d - jnp.minimum(v, 0.0)
    a_s = d + jnp.maximum(v_s, 0.0)
    last_lane = lanes == LANES - 1
    first_lane = lanes == 0
    top_row = rows == 7
    bottom_row = rows == 0
    a_ew = jnp.where(last_lane, a_e, jnp.where(first_lane, a_w, 0.0))
    a_ns = jnp.where(top_row, a_n, jnp.where(bottom_row, a_s, 0.0))
    a_e = jnp.where(last_lane, 0.0, a_e)
    a_w = jnp.where(first_lane, 0.0, a_w)
    a_n = jnp.where(top_row, 0.0, a_n)
    a_s = jnp.where(bottom_row, 0.0, a_s)
    src = sscr[...]
    if with_sends:
        me_ref[...] = jnp.zeros(me_ref.shape, jnp.float32)
        mw_ref[...] = jnp.zeros(mw_ref.shape, jnp.float32)
    for f in range(fields):
        c = x_ref[f]
        halo = _column_matrix(_get_column(fw_ref, f, pieces), _get_column(fe_ref, f, pieces), count)
        hscr[pl.ds(7, levels, stride=8), :] = fn_ref[f]
        hscr[pl.ds(0, levels, stride=8), :] = fs_ref[f]
        hrow = hscr[...]
        out = (a_c * c + a_e * pltpu.roll(c, LANES - 1, 1) + a_w * pltpu.roll(c, 1, 1)
               + a_n * pltpu.roll(c, count - 1, 0) + a_s * pltpu.roll(c, 1, 0)
               + a_ew * halo + a_ns * hrow + coef_ref[f] * src)
        o_ref[f] = out
        if with_sends:
            cols = _columns(out)
            _put_column(me_ref, f, cols[LANES - 1:LANES])
            _put_column(mw_ref, f, cols[0:1])
            sn_ref[f] = o_ref[f, pl.ds(7, levels, stride=8), :]
            ss_ref[f] = o_ref[f, pl.ds(0, levels, stride=8), :]
    if with_sends:
        nxt = step_index + 1
        _send_records(me_ref, prof, mass_new, ie_ref[nxt:nxt + 1, :])
        _send_records(mw_ref, prof, mass_new, iw_ref[nxt:nxt + 1, :])


def _vmem():
    return pl.BlockSpec(memory_space=pltpu.VMEM)


def _f32(shape):
    return jax.ShapeDtypeStruct(shape, jnp.float32)


def prep(x, c, prof, mass, ie, iw):
    fields, count, _ = x.shape
    levels = count // 8
    return pl.pallas_call(
        _prep_kernel,
        out_shape=(
            _f32((fields + 1, levels, LANES)),
            _f32((fields, levels, LANES)),
            _f32((MSG_ROWS, LANES)),
            _f32((MSG_ROWS, LANES)),
        ),
        in_specs=[_vmem()] * 6,
        out_specs=tuple(_vmem() for _ in range(4)),
    )(x, c, prof, mass, ie, iw)


def step(step_index, with_sends, coef, d, x, c, prof, mass, cell, ie, iw, fn, fs, fw, fe, cs, cw):
    fields, count, _ = x.shape
    levels = count // 8
    outs = [_f32(x.shape), _f32(prof.shape), _f32(mass.shape)]
    if with_sends:
        outs += [
            _f32((fields, levels, LANES)),
            _f32((fields, levels, LANES)),
            _f32((MSG_ROWS, LANES)),
            _f32((MSG_ROWS, LANES)),
        ]
    return pl.pallas_call(
        functools.partial(_step_kernel, step_index, with_sends),
        out_shape=tuple(outs),
        in_specs=[pl.BlockSpec(memory_space=pltpu.SMEM)] * 2 + [_vmem()] * 13,
        out_specs=tuple(_vmem() for _ in outs),
        scratch_shapes=[pltpu.VMEM((count, LANES), jnp.float32)] * 3,
    )(coef, d, x, c, prof, mass, cell, ie, iw, fn, fs, fw, fe, cs, cw)


def shift(value, axis, steps, periodic):
    count = lax.axis_size(axis)
    if periodic:
        pairs = [(s, (s + steps) % count) for s in range(count)]
    else:
        pairs = [(s, s + steps) for s in range(count) if 0 <= s + steps < count]
    return lax.ppermute(value, axis, pairs)


def per_device(tracers, courant, diffusivity, melt_coef, berg_profile, berg_mass, berg_cell,
               send_east, send_west):
    fields, levels, rows, cols = tracers.shape
    count = levels * rows
    x = tracers.reshape(fields, count, cols)
    c = courant.reshape(2, count, cols)
    d = diffusivity
    prof = berg_profile
    mass = berg_mass
    sn, ss, me, mw = prep(x, c, prof, mass, send_east, send_west)
    cs = cw = None
    for step_index in range(STEPS):
        from_s = shift(sn, "lat", 1, False)
        from_n = shift(ss, "lat", -1, False)
        from_w = shift(me, "lon", 1, True)
        from_e = shift(mw, "lon", -1, True)
        if cs is None:
            cs, cw = from_s, from_w
        with_sends = step_index < STEPS - 1
        result = step(step_index, with_sends, melt_coef, d, x, c, prof, mass, berg_cell, send_east,
                      send_west, from_n, from_s, from_w, from_e, cs, cw)
        if with_sends:
            x, prof, mass, sn, ss, me, mw = result
        else:
            x, prof, mass = result
    return (x.reshape(fields, levels, rows, cols), mass)


def solution(mesh):
    in_specs = (
        P(None, None, "lat", "lon"),
        P(None, None, "lat", "lon"),
        P(),
        P(),
        P(None, ("lon", "lat")),
        P(("lon", "lat")),
        P(None, ("lon", "lat")),
        P(None, ("lon", "lat")),
        P(None, ("lon", "lat")),
    )
    out_specs = (P(None, None, "lat", "lon"), P(("lon", "lat")))
    return jax.shard_map(
        per_device, mesh=mesh, in_specs=in_specs, out_specs=out_specs, check_vma=False
    )
```

```python
import functools

import jax
import jax.numpy as jnp
from jax import lax
from jax.experimental import pallas as pl
from jax.experimental.pallas import tpu as pltpu
from jax.sharding import PartitionSpec as P

STEPS = 2
LANES = 128
HI = lax.Precision.HIGHEST
REC_ROW = 32
MSG_ROWS = 112


def _dot(a, b, dims):
    return lax.dot_general(a, b, (dims, ((), ())), precision=HI, preferred_element_type=jnp.float32)


def _split3(a):
    hi = a.astype(jnp.bfloat16)
    rest = a - hi.astype(jnp.float32)
    mid = rest.astype(jnp.bfloat16)
    lo = (rest - mid.astype(jnp.float32)).astype(jnp.bfloat16)
    return jnp.concatenate([hi, mid, lo], axis=0)


def _select(a, hot, dims):
    m = a.shape[0]
    part = lax.dot_general(_split3(a), hot.astype(jnp.bfloat16), (dims, ((), ())),
                           preferred_element_type=jnp.float32)
    return (part[:m] + part[m:2 * m]) + part[2 * m:]


def _pieces(count):
    return -(-count // LANES)


def _columns(block):
    count = block.shape[0]
    width = _pieces(count) * LANES
    padded = jnp.concatenate([block, jnp.zeros((width - count, LANES), jnp.float32)], axis=0)
    return padded.T


def _put_column(msg_ref, slot, vector):
    pieces = vector.shape[1] // LANES
    for j in range(pieces):
        row = slot * pieces + j
        msg_ref[pl.ds(row, 1), :] = vector[:, j * LANES:(j + 1) * LANES]


def _get_column(msg_ref, slot, pieces):
    return jnp.concatenate(
        [msg_ref[pl.ds(slot * pieces + j, 1), :] for j in range(pieces)], axis=1)


def _column_matrix(west, east, count):
    width = west.shape[-1]
    r = lax.broadcasted_iota(jnp.int32, (LANES, width), 0)
    grid = jnp.where(r == 0, west, jnp.where(r == LANES - 1, east, 0.0))
    return grid.T[:count]


def _one_hot(index_row, size):
    n = index_row.shape[1]
    return jnp.where(lax.broadcasted_iota(jnp.int32, (size, n), 0) == index_row, 1.0, 0.0)


def _send_records(msg_ref, prof, mass, index_row):
    slots = prof.shape[1]
    hot = _one_hot(index_row, slots)
    levels = prof.shape[0]
    cross = index_row.shape[1]
    rec = _select(jnp.concatenate([prof, mass, jnp.zeros((4, slots), jnp.float32)], axis=0), hot,
                  ((1,), (0,)))
    msg_ref[REC_ROW:REC_ROW + levels + 1, 0:cross] = rec[:levels + 1]


def _prep_kernel(fields, x_ref, c_ref, p_ref, m_ref, ie_ref, iw_ref, sn_ref, ss_ref, me_ref, mw_ref):
    f = pl.program_id(0)
    count = x_ref.shape[1]
    levels = count // 8

    @pl.when(f == 0)
    def _():
        me_ref[...] = jnp.zeros(me_ref.shape, jnp.float32)
        mw_ref[...] = jnp.zeros(mw_ref.shape, jnp.float32)
        ucols = _columns(c_ref[0])
        _put_column(me_ref, fields, ucols[LANES - 1:LANES])
        sn_ref[fields] = c_ref[1, pl.ds(7, levels, stride=8), :]
        prof = p_ref[...]
        mass = m_ref[...].reshape(1, -1)
        _send_records(me_ref, prof, mass, ie_ref[0:1, :])
        _send_records(mw_ref, prof, mass, iw_ref[0:1, :])

    cols = _columns(x_ref[0])
    _put_column(me_ref, f, cols[LANES - 1:LANES])
    _put_column(mw_ref, f, cols[0:1])
    sn_ref[f] = x_ref[0, pl.ds(7, levels, stride=8), :]
    ss_ref[f] = x_ref[0, pl.ds(0, levels, stride=8), :]


def _step_kernel(fields, step_index, with_sends, coef_ref, d_ref, x_ref, c_ref, p_ref, m_ref, cell_ref,
                 ie_ref, iw_ref, fn_ref, fs_ref, fw_ref, fe_ref, cs_ref, cw_ref, *rest):
    if with_sends:
        o_ref, po_ref, mo_ref, sn_ref, ss_ref, me_ref, mw_ref = rest[:7]
    else:
        o_ref, po_ref, mo_ref = rest[:3]
    hscr, sscr, dscr, k_c, k_e, k_w, k_n, k_s, k_ew, k_ns = rest[-10:]
    f = pl.program_id(0)
    count = x_ref.shape[1]
    levels = count // 8
    pieces = _pieces(count)
    slots = p_ref.shape[1]
    cross = ie_ref.shape[1]
    cells = 8 * LANES

    @pl.when(f == 0)
    def _():
        hot_e = _one_hot(ie_ref[step_index:step_index + 1, :], slots)
        hot_w = _one_hot(iw_ref[step_index:step_index + 1, :], slots)
        rec_e = fw_ref[REC_ROW:REC_ROW + levels + 5, 0:cross]
        rec_w = fe_ref[REC_ROW:REC_ROW + levels + 5, 0:cross]
        placed = _select(rec_e, hot_e, ((1,), (1,))) + _select(rec_w, hot_w, ((1,), (1,)))
        taken = lax.dot_general(jnp.ones((8, cross), jnp.bfloat16), (hot_e + hot_w).astype(jnp.bfloat16),
                                (((1,), (1,)), ((), ())), preferred_element_type=jnp.float32)[0:1]
        moved = taken > 0.5
        prof = jnp.where(moved, placed[:levels], p_ref[...])
        mass = jnp.where(moved, placed[levels:levels + 1], m_ref[...].reshape(1, -1))

        temp = jnp.concatenate([x_ref[0, pl.ds(r, levels, stride=8), :] for r in range(8)], axis=1)
        hot_c = _one_hot(cell_ref[step_index:step_index + 1, :], cells)
        water = _select(temp, hot_c, ((1,), (0,)))
        z = water + 1.8
        soft = jnp.maximum(z, 0.0) + jnp.log1p(jnp.exp(-jnp.abs(z)))
        melt = prof * soft * jnp.sqrt(mass)
        source = _select(melt, hot_c, ((1,), (1,)))
        mass_new = mass / (1.0 + 0.05 * jnp.sum(melt, axis=0, keepdims=True))
        po_ref[...] = prof
        mo_ref[...] = mass_new.reshape(-1)
        for r in range(8):
            sscr[pl.ds(r, levels, stride=8), :] = source[:, r * LANES:(r + 1) * LANES]
        for l in range(levels):
            dscr[l * 8:(l + 1) * 8, :] = jnp.full((8, LANES), d_ref[l], jnp.float32)

        rows = lax.broadcasted_iota(jnp.int32, (count, LANES), 0) % 8
        lanes = lax.broadcasted_iota(jnp.int32, (count, LANES), 1)
        u = c_ref[0]
        v = c_ref[1]
        d = dscr[...]
        zero_row = jnp.zeros((1, pieces * LANES), jnp.float32)
        u_halo = _column_matrix(_get_column(cw_ref, fields, pieces), zero_row, count)
        u_w = jnp.where(lanes == 0, u_halo, pltpu.roll(u, 1, 1))
        hscr[...] = jnp.zeros(hscr.shape, jnp.float32)
        hscr[pl.ds(0, levels, stride=8), :] = cs_ref[0]
        v_s = jnp.where(rows == 0, hscr[...], pltpu.roll(v, 1, 0))
        a_c = 1.0 - jnp.maximum(u, 0.0) + jnp.minimum(u_w, 0.0) - jnp.maximum(v, 0.0) + jnp.minimum(v_s, 0.0) - 4.0 * d
        a_e = d - jnp.minimum(u, 0.0)
        a_w = d + jnp.maximum(u_w, 0.0)
        a_n = d - jnp.minimum(v, 0.0)
        a_s = d + jnp.maximum(v_s, 0.0)
        last_lane = lanes == LANES - 1
        first_lane = lanes == 0
        top_row = rows == 7
        bottom_row = rows == 0
        k_c[...] = a_c
        k_ew[...] = jnp.where(last_lane, a_e, jnp.where(first_lane, a_w, 0.0))
        k_ns[...] = jnp.where(top_row, a_n, jnp.where(bottom_row, a_s, 0.0))
        k_e[...] = jnp.where(last_lane, 0.0, a_e)
        k_w[...] = jnp.where(first_lane, 0.0, a_w)
        k_n[...] = jnp.where(top_row, 0.0, a_n)
        k_s[...] = jnp.where(bottom_row, 0.0, a_s)
        if with_sends:
            me_ref[...] = jnp.zeros(me_ref.shape, jnp.float32)
            mw_ref[...] = jnp.zeros(mw_ref.shape, jnp.float32)
            nxt = step_index + 1
            _send_records(me_ref, prof, mass_new, ie_ref[nxt:nxt + 1, :])
            _send_records(mw_ref, prof, mass_new, iw_ref[nxt:nxt + 1, :])

    c = x_ref[0]
    halo = _column_matrix(_get_column(fw_ref, f, pieces), _get_column(fe_ref, f, pieces), count)
    hscr[pl.ds(7, levels, stride=8), :] = fn_ref[0]
    hscr[pl.ds(0, levels, stride=8), :] = fs_ref[0]
    hrow = hscr[...]
    out = (k_c[...] * c + k_e[...] * pltpu.roll(c, LANES - 1, 1) + k_w[...] * pltpu.roll(c, 1, 1)
           + k_n[...] * pltpu.roll(c, count - 1, 0) + k_s[...] * pltpu.roll(c, 1, 0)
           + k_ew[...] * halo + k_ns[...] * hrow + coef_ref[f] * sscr[...])
    o_ref[0] = out
    if with_sends:
        cols = _columns(out)
        _put_column(me_ref, f, cols[LANES - 1:LANES])
        _put_column(mw_ref, f, cols[0:1])
        sn_ref[0] = o_ref[0, pl.ds(7, levels, stride=8), :]
        ss_ref[0] = o_ref[0, pl.ds(0, levels, stride=8), :]


def _vmem():
    return pl.BlockSpec(memory_space=pltpu.VMEM)


def _f32(shape):
    return jax.ShapeDtypeStruct(shape, jnp.float32)


def _whole(shape):
    return pl.BlockSpec(shape, lambda f: (0,) * len(shape))


def _field(shape):
    return pl.BlockSpec((1,) + tuple(shape[1:]), lambda f: (f,) + (0,) * (len(shape) - 1))


def prep(x, c, prof, mass, ie, iw):
    fields, count, _ = x.shape
    levels = count // 8
    out_shape = (
        _f32((fields + 1, levels, LANES)),
        _f32((fields, levels, LANES)),
        _f32((MSG_ROWS, LANES)),
        _f32((MSG_ROWS, LANES)),
    )
    return pl.pallas_call(
        functools.partial(_prep_kernel, fields),
        grid=(fields,),
        out_shape=out_shape,
        in_specs=[_field(x.shape)] + [_whole(a.shape) for a in (c, prof, mass, ie, iw)],
        out_specs=tuple(_whole(o.shape) for o in out_shape),
    )(x, c, prof, mass, ie, iw)


def step(step_index, with_sends, coef, d, x, c, prof, mass, cell, ie, iw, fn, fs, fw, fe, cs, cw):
    fields, count, _ = x.shape
    levels = count // 8
    outs = [_f32(x.shape), _f32(prof.shape), _f32(mass.shape)]
    out_specs = [_field(x.shape), _whole(prof.shape), _whole(mass.shape)]
    if with_sends:
        outs += [
            _f32((fields, levels, LANES)),
            _f32((fields, levels, LANES)),
            _f32((MSG_ROWS, LANES)),
            _f32((MSG_ROWS, LANES)),
        ]
        out_specs += [_field(outs[3].shape), _field(outs[4].shape), _whole(outs[5].shape),
                      _whole(outs[6].shape)]
    smem = pl.BlockSpec(memory_space=pltpu.SMEM)
    in_specs = [smem, smem, _field(x.shape)] + [_whole(a.shape) for a in (c, prof, mass, cell, ie, iw)]
    in_specs += [_field(fn.shape), _field(fs.shape), _whole(fw.shape), _whole(fe.shape),
                 pl.BlockSpec((1, levels, LANES), lambda f: (fields, 0, 0)), _whole(cw.shape)]
    return pl.pallas_call(
        functools.partial(_step_kernel, fields, step_index, with_sends),
        grid=(fields,),
        out_shape=tuple(outs),
        in_specs=in_specs,
        out_specs=tuple(out_specs),
        scratch_shapes=[pltpu.VMEM((count, LANES), jnp.float32)] * 10,
    )(coef, d, x, c, prof, mass, cell, ie, iw, fn, fs, fw, fe, cs, cw)


def shift(value, axis, steps, periodic):
    count = lax.axis_size(axis)
    if periodic:
        pairs = [(s, (s + steps) % count) for s in range(count)]
    else:
        pairs = [(s, s + steps) for s in range(count) if 0 <= s + steps < count]
    return lax.ppermute(value, axis, pairs)


def per_device(tracers, courant, diffusivity, melt_coef, berg_profile, berg_mass, berg_cell,
               send_east, send_west):
    fields, levels, rows, cols = tracers.shape
    count = levels * rows
    x = tracers.reshape(fields, count, cols)
    c = courant.reshape(2, count, cols)
    d = diffusivity
    prof = berg_profile
    mass = berg_mass
    sn, ss, me, mw = prep(x, c, prof, mass, send_east, send_west)
    cs = cw = None
    for step_index in range(STEPS):
        from_s = shift(sn, "lat", 1, False)
        from_n = shift(ss, "lat", -1, False)
        from_w = shift(me, "lon", 1, True)
        from_e = shift(mw, "lon", -1, True)
        if cs is None:
            cs, cw = from_s, from_w
        with_sends = step_index < STEPS - 1
        result = step(step_index, with_sends, melt_coef, d, x, c, prof, mass, berg_cell, send_east,
                      send_west, from_n, from_s, from_w, from_e, cs, cw)
        if with_sends:
            x, prof, mass, sn, ss, me, mw = result
        else:
            x, prof, mass = result
    return (x.reshape(fields, levels, rows, cols), mass)


def solution(mesh):
    in_specs = (
        P(None, None, "lat", "lon"),
        P(None, None, "lat", "lon"),
        P(),
        P(),
        P(None, ("lon", "lat")),
        P(("lon", "lat")),
        P(None, ("lon", "lat")),
        P(None, ("lon", "lat")),
        P(None, ("lon", "lat")),
    )
    out_specs = (P(None, None, "lat", "lon"), P(("lon", "lat")))
    return jax.shard_map(
        per_device, mesh=mesh, in_specs=in_specs, out_specs=out_specs, check_vma=False
    )
```

```python
import functools

import jax
import jax.numpy as jnp
from jax import lax
from jax.experimental import pallas as pl
from jax.experimental.pallas import tpu as pltpu
from jax.sharding import PartitionSpec as P

STEPS = 2
LANES = 128
HI = lax.Precision.HIGHEST
REC_ROW = 32
MSG_ROWS = 112


def _dot(a, b, dims):
    return lax.dot_general(a, b, (dims, ((), ())), precision=HI, preferred_element_type=jnp.float32)


def _split3(a):
    hi = a.astype(jnp.bfloat16)
    rest = a - hi.astype(jnp.float32)
    mid = rest.astype(jnp.bfloat16)
    lo = (rest - mid.astype(jnp.float32)).astype(jnp.bfloat16)
    return jnp.concatenate([hi, mid, lo], axis=0)


def _select(a, hot, dims):
    m = a.shape[0]
    part = lax.dot_general(_split3(a), hot.astype(jnp.bfloat16), (dims, ((), ())),
                           preferred_element_type=jnp.float32)
    return (part[:m] + part[m:2 * m]) + part[2 * m:]


def _pieces(count):
    return -(-count // LANES)


def _columns(block):
    count = block.shape[0]
    width = _pieces(count) * LANES
    padded = jnp.concatenate([block, jnp.zeros((width - count, LANES), jnp.float32)], axis=0)
    return padded.T


def _put_column(msg_ref, slot, vector):
    pieces = vector.shape[1] // LANES
    for j in range(pieces):
        row = slot * pieces + j
        msg_ref[row:row + 1, :] = vector[:, j * LANES:(j + 1) * LANES]


def _get_column(msg_ref, slot, pieces):
    return jnp.concatenate(
        [msg_ref[slot * pieces + j:slot * pieces + j + 1, :] for j in range(pieces)], axis=1)


def _column_matrix(west, east, count):
    width = west.shape[-1]
    r = lax.broadcasted_iota(jnp.int32, (LANES, width), 0)
    grid = jnp.where(r == 0, west, jnp.where(r == LANES - 1, east, 0.0))
    return grid.T[:count]


def _one_hot(index_row, size):
    n = index_row.shape[1]
    return jnp.where(lax.broadcasted_iota(jnp.int32, (size, n), 0) == index_row, 1.0, 0.0)


def _send_records(msg_ref, prof, mass, index_row):
    slots = prof.shape[1]
    hot = _one_hot(index_row, slots)
    levels = prof.shape[0]
    cross = index_row.shape[1]
    rec = _select(jnp.concatenate([prof, mass, jnp.zeros((4, slots), jnp.float32)], axis=0), hot,
                  ((1,), (0,)))
    msg_ref[REC_ROW:REC_ROW + levels + 1, 0:cross] = rec[:levels + 1]


def _prep_kernel(x_ref, c_ref, p_ref, m_ref, ie_ref, iw_ref, sn_ref, ss_ref, me_ref, mw_ref):
    fields, count, _ = x_ref.shape
    levels = count // 8
    me_ref[...] = jnp.zeros(me_ref.shape, jnp.float32)
    mw_ref[...] = jnp.zeros(mw_ref.shape, jnp.float32)
    for f in range(fields):
        cols = _columns(x_ref[f])
        _put_column(me_ref, f, cols[LANES - 1:LANES])
        _put_column(mw_ref, f, cols[0:1])
        sn_ref[f] = x_ref[f, pl.ds(7, levels, stride=8), :]
        ss_ref[f] = x_ref[f, pl.ds(0, levels, stride=8), :]
    ucols = _columns(c_ref[0])
    _put_column(me_ref, fields, ucols[LANES - 1:LANES])
    sn_ref[fields] = c_ref[1, pl.ds(7, levels, stride=8), :]
    prof = p_ref[...]
    mass = m_ref[...].reshape(1, -1)
    _send_records(me_ref, prof, mass, ie_ref[0:1, :])
    _send_records(mw_ref, prof, mass, iw_ref[0:1, :])


def _step_kernel(step_index, with_sends, coef_ref, d_ref, p_ref, m_ref, cell_ref, ie_ref, iw_ref,
                 x_hbm, c_hbm, fn_hbm, fs_hbm, fw_hbm, fe_hbm, cs_hbm, cw_hbm, *rest):
    if with_sends:
        o_hbm, po_ref, mo_ref, sn_ref, ss_ref, me_ref, mw_ref = rest[:7]
    else:
        o_hbm, po_ref, mo_ref = rest[:3]
    (xv, cv, fnv, fsv, fwv, fev, csv, cwv, ov, hscr, sscr, dscr, sem) = rest[-13:]
    fields, count, _ = xv.shape
    levels = count // 8
    pieces = _pieces(count)
    slots = p_ref.shape[1]
    cross = ie_ref.shape[1]
    cells = 8 * LANES

    def fetch(src, dst, k):
        cp = pltpu.make_async_copy(src, dst, sem.at[k])
        cp.start()
        return cp

    c_fw = fetch(fw_hbm, fwv, 0)
    c_fe = fetch(fe_hbm, fev, 1)
    c_x = [fetch(x_hbm.at[0], xv.at[0], 2)]
    c_c = fetch(c_hbm, cv, 3)
    c_cs = fetch(cs_hbm.at[fields], csv, 4)
    c_cw = fetch(cw_hbm, cwv, 5)
    c_fn = fetch(fn_hbm, fnv, 6)
    c_fs = fetch(fs_hbm.at[pl.ds(0, fields)], fsv, 7)
    for f in range(1, fields):
        c_x.append(fetch(x_hbm.at[f], xv.at[f], 7 + f))

    c_fw.wait()
    c_fe.wait()
    hot_e = _one_hot(ie_ref[step_index:step_index + 1, :], slots)
    hot_w = _one_hot(iw_ref[step_index:step_index + 1, :], slots)
    rec_e = fwv[REC_ROW:REC_ROW + levels + 5, 0:cross]
    rec_w = fev[REC_ROW:REC_ROW + levels + 5, 0:cross]
    placed = _select(rec_e, hot_e, ((1,), (1,))) + _select(rec_w, hot_w, ((1,), (1,)))
    taken = lax.dot_general(jnp.ones((8, cross), jnp.bfloat16), (hot_e + hot_w).astype(jnp.bfloat16),
                            (((1,), (1,)), ((), ())), preferred_element_type=jnp.float32)[0:1]
    moved = taken > 0.5
    prof = jnp.where(moved, placed[:levels], p_ref[...])
    mass = jnp.where(moved, placed[levels:levels + 1], m_ref[...].reshape(1, -1))

    c_x[0].wait()
    temp = jnp.concatenate([xv[0, pl.ds(r, levels, stride=8), :] for r in range(8)], axis=1)
    hot_c = _one_hot(cell_ref[step_index:step_index + 1, :], cells)
    water = _select(temp, hot_c, ((1,), (0,)))
    z = water + 1.8
    soft = jnp.maximum(z, 0.0) + jnp.log1p(jnp.exp(-jnp.abs(z)))
    melt = prof * soft * jnp.sqrt(mass)
    source = _select(melt, hot_c, ((1,), (1,)))
    mass_new = mass / (1.0 + 0.05 * jnp.sum(melt, axis=0, keepdims=True))
    po_ref[...] = prof
    mo_ref[...] = mass_new.reshape(-1)
    for r in range(8):
        sscr[pl.ds(r, levels, stride=8), :] = source[:, r * LANES:(r + 1) * LANES]
    for l in range(levels):
        dscr[l * 8:(l + 1) * 8, :] = jnp.full((8, LANES), d_ref[l], jnp.float32)
    if with_sends:
        me_ref[...] = jnp.zeros(me_ref.shape, jnp.float32)
        mw_ref[...] = jnp.zeros(mw_ref.shape, jnp.float32)
        nxt = step_index + 1
        _send_records(me_ref, prof, mass_new, ie_ref[nxt:nxt + 1, :])
        _send_records(mw_ref, prof, mass_new, iw_ref[nxt:nxt + 1, :])

    c_c.wait()
    c_cs.wait()
    c_cw.wait()
    rows = lax.broadcasted_iota(jnp.int32, (count, LANES), 0) % 8
    lanes = lax.broadcasted_iota(jnp.int32, (count, LANES), 1)
    u = cv[0]
    v = cv[1]
    d = dscr[...]
    zero_row = jnp.zeros((1, pieces * LANES), jnp.float32)
    u_halo = _column_matrix(_get_column(cwv, fields, pieces), zero_row, count)
    u_w = jnp.where(lanes == 0, u_halo, pltpu.roll(u, 1, 1))
    hscr[...] = jnp.zeros(hscr.shape, jnp.float32)
    hscr[pl.ds(0, levels, stride=8), :] = csv[...]
    v_s = jnp.where(rows == 0, hscr[...], pltpu.roll(v, 1, 0))
    a_c = 1.0 - jnp.maximum(u, 0.0) + jnp.minimum(u_w, 0.0) - jnp.maximum(v, 0.0) + jnp.minimum(v_s, 0.0) - 4.0 * d
    a_e = d - jnp.minimum(u, 0.0)
    a_w = d + jnp.maximum(u_w, 0.0)
    a_n = d - jnp.minimum(v, 0.0)
    a_s = d + jnp.maximum(v_s, 0.0)
    last_lane = lanes == LANES - 1
    first_lane = lanes == 0
    top_row = rows == 7
    bottom_row = rows == 0
    a_ew = jnp.where(last_lane, a_e, jnp.where(first_lane, a_w, 0.0))
    a_ns = jnp.where(top_row, a_n, jnp.where(bottom_row, a_s, 0.0))
    a_e = jnp.where(last_lane, 0.0, a_e)
    a_w = jnp.where(first_lane, 0.0, a_w)
    a_n = jnp.where(top_row, 0.0, a_n)
    a_s = jnp.where(bottom_row, 0.0, a_s)
    src = sscr[...]
    c_fn.wait()
    c_fs.wait()
    outs = []
    for f in range(fields):
        if f > 0:
            c_x[f].wait()
        c = xv[f]
        halo = _column_matrix(_get_column(fwv, f, pieces), _get_column(fev, f, pieces), count)
        hscr[pl.ds(7, levels, stride=8), :] = fnv[f]
        hscr[pl.ds(0, levels, stride=8), :] = fsv[f]
        hrow = hscr[...]
        out = (a_c * c + a_e * pltpu.roll(c, LANES - 1, 1) + a_w * pltpu.roll(c, 1, 1)
               + a_n * pltpu.roll(c, count - 1, 0) + a_s * pltpu.roll(c, 1, 0)
               + a_ew * halo + a_ns * hrow + coef_ref[f] * src)
        ov[f] = out
        cp = pltpu.make_async_copy(ov.at[f], o_hbm.at[f], sem.at[7 + fields + f])
        cp.start()
        outs.append(cp)
        if with_sends:
            cols = _columns(out)
            _put_column(me_ref, f, cols[LANES - 1:LANES])
            _put_column(mw_ref, f, cols[0:1])
            sn_ref[f] = ov[f, pl.ds(7, levels, stride=8), :]
            ss_ref[f] = ov[f, pl.ds(0, levels, stride=8), :]
    for cp in outs:
        cp.wait()


def _vmem():
    return pl.BlockSpec(memory_space=pltpu.VMEM)


def _f32(shape):
    return jax.ShapeDtypeStruct(shape, jnp.float32)


def prep(x, c, prof, mass, ie, iw):
    fields, count, _ = x.shape
    levels = count // 8
    return pl.pallas_call(
        _prep_kernel,
        out_shape=(
            _f32((fields + 1, levels, LANES)),
            _f32((fields, levels, LANES)),
            _f32((MSG_ROWS, LANES)),
            _f32((MSG_ROWS, LANES)),
        ),
        in_specs=[_vmem()] * 6,
        out_specs=tuple(_vmem() for _ in range(4)),
    )(x, c, prof, mass, ie, iw)


def step(step_index, with_sends, coef, d, x, c, prof, mass, cell, ie, iw, fn, fs, fw, fe, cs, cw):
    fields, count, _ = x.shape
    levels = count // 8
    anyspace = pl.BlockSpec(memory_space=pl.ANY)
    outs = [_f32(x.shape), _f32(prof.shape), _f32(mass.shape)]
    out_specs = [anyspace, _vmem(), _vmem()]
    if with_sends:
        outs += [
            _f32((fields, levels, LANES)),
            _f32((fields, levels, LANES)),
            _f32((MSG_ROWS, LANES)),
            _f32((MSG_ROWS, LANES)),
        ]
        out_specs += [_vmem()] * 4
    smem = pl.BlockSpec(memory_space=pltpu.SMEM)
    scratch = [
        pltpu.VMEM(x.shape, jnp.float32),
        pltpu.VMEM(c.shape, jnp.float32),
        pltpu.VMEM((fields, levels, LANES), jnp.float32),
        pltpu.VMEM((fields, levels, LANES), jnp.float32),
        pltpu.VMEM(fw.shape, jnp.float32),
        pltpu.VMEM(fe.shape, jnp.float32),
        pltpu.VMEM((levels, LANES), jnp.float32),
        pltpu.VMEM(cw.shape, jnp.float32),
        pltpu.VMEM(x.shape, jnp.float32),
        pltpu.VMEM((count, LANES), jnp.float32),
        pltpu.VMEM((count, LANES), jnp.float32),
        pltpu.VMEM((count, LANES), jnp.float32),
        pltpu.SemaphoreType.DMA((7 + 2 * fields,)),
    ]
    return pl.pallas_call(
        functools.partial(_step_kernel, step_index, with_sends),
        out_shape=tuple(outs),
        in_specs=[smem, smem] + [_vmem()] * 5 + [anyspace] * 8,
        out_specs=tuple(out_specs),
        scratch_shapes=scratch,
    )(coef, d, prof, mass, cell, ie, iw, x, c, fn, fs, fw, fe, cs, cw)


def shift(value, axis, steps, periodic):
    count = lax.axis_size(axis)
    if periodic:
        pairs = [(s, (s + steps) % count) for s in range(count)]
    else:
        pairs = [(s, s + steps) for s in range(count) if 0 <= s + steps < count]
    return lax.ppermute(value, axis, pairs)


def per_device(tracers, courant, diffusivity, melt_coef, berg_profile, berg_mass, berg_cell,
               send_east, send_west):
    fields, levels, rows, cols = tracers.shape
    count = levels * rows
    x = tracers.reshape(fields, count, cols)
    c = courant.reshape(2, count, cols)
    d = diffusivity
    prof = berg_profile
    mass = berg_mass
    sn, ss, me, mw = prep(x, c, prof, mass, send_east, send_west)
    cs = cw = None
    for step_index in range(STEPS):
        from_s = shift(sn, "lat", 1, False)
        from_n = shift(ss, "lat", -1, False)
        from_w = shift(me, "lon", 1, True)
        from_e = shift(mw, "lon", -1, True)
        if cs is None:
            cs, cw = from_s, from_w
        with_sends = step_index < STEPS - 1
        result = step(step_index, with_sends, melt_coef, d, x, c, prof, mass, berg_cell, send_east,
                      send_west, from_n, from_s, from_w, from_e, cs, cw)
        if with_sends:
            x, prof, mass, sn, ss, me, mw = result
        else:
            x, prof, mass = result
    return (x.reshape(fields, levels, rows, cols), mass)


def solution(mesh):
    in_specs = (
        P(None, None, "lat", "lon"),
        P(None, None, "lat", "lon"),
        P(),
        P(),
        P(None, ("lon", "lat")),
        P(("lon", "lat")),
        P(None, ("lon", "lat")),
        P(None, ("lon", "lat")),
        P(None, ("lon", "lat")),
    )
    out_specs = (P(None, None, "lat", "lon"), P(("lon", "lat")))
    return jax.shard_map(
        per_device, mesh=mesh, in_specs=in_specs, out_specs=out_specs, check_vma=False
    )
```
